1024 devices in a mesh: ctx: 16 (over y, x), tp: 64 (over z, core).
Axes of the slice: x: 4, y: 4, z: 32, core: 2. Of those that a mesh axis runs over, the one named last changes fastest.
Arguments:
- tokens: bfloat16 [2048, 16384], P(None, 'ctx'), may hold values from -4 to 4
- wq: bfloat16 [16384, 16384], P('ctx', 'tp'), may hold values from -0.046875 to 0.046875
- wk: bfloat16 [16384, 1024], P('ctx', 'tp'), may hold values from -0.046875 to 0.046875
- wv: bfloat16 [16384, 1024], P('ctx', 'tp'), may hold values from -0.046875 to 0.046875
- doc_len: int32 [64], replicated, may hold values from 1 to 189, as said below
- doc_shard: int32 [64], replicated, may hold values from 0 to 15, as said below
- doc_slot: int32 [64], replicated, may hold values from 0 to 191, as said below
Outputs:
- attended: bfloat16 [3072, 16384], P('ctx', 'tp')
The draws below stay inside these ranges and needn't reach their ends.
Inputs may be any that keep to these rules, and one draw needn't show every extreme that they name: `doc_len`: documents lie in the packed sequence in index order and their lengths sum to 2048; in every draw some document has length 189. `doc_shard`: each shard holds exactly 4 documents whose lengths sum to at most 192; in every draw some shard holds exactly 192 tokens. The documents of one shard take disjoint runs of slots doc_slot to doc_slot + doc_len - 1, filling the slots from 0 without gaps; in every draw some document starts at slot 191.
All inputs are finite; a program needn't handle non-finite values.
Results may differ from the reference program's by a relative error of at most 0.035.
Values may be sent and summed in bfloat16 or wider, within the bound.
No kernel may reach another device: no remote copies, remote signals or barrier semaphores. Data moves between devices by JAX's collectives and lax.ppermute only.
A program may use at most 32 MiB of HBM per device.

```python
import jax
import jax.numpy as jnp
from jax import lax

MODEL_WIDTH = 16384
QUERY_HEADS = 128
KEY_VALUE_HEADS = 8
HEAD_SIZE = 128
TOK_CTX = 128
DPS = 4
SHARD_SLOT_COUNT = 192
TOKENS = 2048
SLOT_COUNT_ALL = 3072
NDOC = 64
N_CTX = 16


def shard_layout(key):
    keys = jax.random.split(jax.random.fold_in(key, 7), 5)
    pairs = N_CTX // 2
    spare = SHARD_SLOT_COUNT - TOK_CTX
    delta = jax.random.randint(keys[0], (pairs,), 0, spare + 1)
    forced = jax.random.randint(keys[1], (), 0, pairs)
    delta = jnp.where(jnp.arange(pairs) == forced, spare, delta)
    flip = jax.random.randint(keys[2], (pairs,), 0, 2)
    first = TOK_CTX + jnp.where(flip == 1, delta, -delta)
    second = 2 * TOK_CTX - first
    counts = jnp.stack([first, second], axis=1).reshape(N_CTX).astype(jnp.int32)
    raw = jax.random.randint(keys[3], (N_CTX, DPS - 1), 0, 1 << 20)
    raw = raw % (counts[:, None] - DPS + 1)
    cuts = jnp.sort(raw, axis=1) + jnp.arange(1, DPS, dtype=jnp.int32)[None, :]
    full_cuts = (SHARD_SLOT_COUNT - DPS + 1 + jnp.arange(0, DPS - 1, dtype=jnp.int32))[None, :]
    cuts = jnp.where(counts[:, None] == SHARD_SLOT_COUNT, full_cuts, cuts).astype(jnp.int32)
    bounds = jnp.concatenate([jnp.zeros((N_CTX, 1), jnp.int32), cuts, counts[:, None]], axis=1)
    lengths = bounds[:, 1:] - bounds[:, :-1]
    offsets = bounds[:, :-1]
    order = jax.random.permutation(keys[4], NDOC)
    doc_len = lengths.reshape(NDOC)[order].astype(jnp.int32)
    doc_shard = (jnp.arange(NDOC, dtype=jnp.int32) // DPS)[order]
    doc_slot = offsets.reshape(NDOC)[order].astype(jnp.int32)
    return (doc_len, doc_shard, doc_slot)


def draw_doc_len(key, part):
    return shard_layout(key)[0]


def draw_doc_shard(key, part):
    return shard_layout(key)[1]


def draw_doc_slot(key, part):
    return shard_layout(key)[2]


def draw_tokens(key, part):
    keys = jax.random.split(jax.random.fold_in(key, 11), 1)
    values = jnp.clip(jax.random.normal(keys[0], (TOKENS, MODEL_WIDTH), jnp.float32), -4.0, 4.0)
    return values.astype(jnp.bfloat16)


def block_scale(own_key, dims, cuts, smallest, high):
    factor_of, own = 1.0, jax.random.fold_in(own_key, 6)
    for dim, parts in cuts:
        draws = jnp.exp(jax.random.uniform(jax.random.fold_in(own, dim), (parts,), jnp.float32, smallest / len(cuts), high / len(cuts)))
        factor_of = factor_of * jnp.repeat(draws, dims[dim] // parts).reshape([-1 if axis == dim else 1 for axis in range(len(dims))])
    return factor_of


def bell_draw(own_key, shape, scale, reach, pieces=(), kind=jnp.bfloat16):
    array = jax.random.normal(own_key, shape, jnp.float32) * scale
    if len(pieces) > 0:
        array = block_scale(own_key, shape, pieces, -0.22, 0.18) * array
    return jnp.clip(array, min=-reach, max=reach).astype(kind)


def setup_inputs(seed: int = 0) -> dict:
    arg_keys = jax.random.split(jax.random.key(seed), 8)
    return {
        "tokens": draw_tokens(jax.random.fold_in(arg_keys[7], 71), 0),
        "wq": bell_draw(arg_keys[1], (MODEL_WIDTH, QUERY_HEADS * HEAD_SIZE), MODEL_WIDTH ** -0.5, 0.046875, ((0, 16), (1, 64))),
        "wk": bell_draw(arg_keys[2], (MODEL_WIDTH, KEY_VALUE_HEADS * HEAD_SIZE), MODEL_WIDTH ** -0.5, 0.046875, ((0, 16), (1, 64))),
        "wv": bell_draw(arg_keys[3], (MODEL_WIDTH, KEY_VALUE_HEADS * HEAD_SIZE), MODEL_WIDTH ** -0.5, 0.046875, ((0, 16), (1, 64))),
        "doc_len": draw_doc_len(jax.random.fold_in(arg_keys[7], 71), 0),
        "doc_shard": draw_doc_shard(jax.random.fold_in(arg_keys[7], 71), 0),
        "doc_slot": draw_doc_slot(jax.random.fold_in(arg_keys[7], 71), 0),
    }


rope_base = 500000.0


def slot_layout(doc_len, doc_shard, doc_slot, tokens_total, capacity, slot_total):
    ends = jnp.cumsum(doc_len).astype(jnp.int32)
    starts = (ends - doc_len).astype(jnp.int32)
    token_ids = jnp.arange(tokens_total, dtype=jnp.int32)
    inside = (token_ids[:, None] >= starts[None, :]) & (token_ids[:, None] < ends[None, :])
    doc_ids = jnp.arange(doc_len.shape[0], dtype=jnp.int32)
    doc_of = jnp.sum(jnp.where(inside, doc_ids[None, :], 0), axis=1).astype(jnp.int32)
    first = jnp.sum(jnp.where(inside, starts[None, :], 0), axis=1).astype(jnp.int32)
    anchor = (doc_shard * capacity + doc_slot).astype(jnp.int32)
    base = jnp.sum(jnp.where(inside, anchor[None, :], 0), axis=1).astype(jnp.int32)
    position = (token_ids - first).astype(jnp.int32)
    target = (base + position).astype(jnp.int32)
    slot_ids = jnp.arange(slot_total, dtype=jnp.int32)
    source = jnp.zeros((slot_total,), jnp.int32).at[target].set(token_ids)
    filled = jnp.zeros((slot_total,), jnp.int32).at[target].set(1)
    slot_doc = jnp.zeros((slot_total,), jnp.int32).at[target].set(doc_of)
    slot_doc = jnp.where(filled == 1, slot_doc, -1 - slot_ids).astype(jnp.int32)
    slot_position_index = jnp.zeros((slot_total,), jnp.int32).at[target].set(position)
    return source, filled, slot_doc, slot_position_index


def apply_rotary(values, positions):
    head_dim = values.shape[-1]
    half = head_dim // 2
    freq = jnp.power(jnp.float32(rope_base), -jnp.arange(half, dtype=jnp.float32) * (2.0 / head_dim))
    angle = positions.astype(jnp.float32)[:, None] * freq[None, :]
    cosine = jnp.cos(angle)[:, None, :]
    sine = jnp.sin(angle)[:, None, :]
    lower = values[..., :half]
    upper = values[..., half:]
    return jnp.concatenate([lower * cosine - upper * sine, upper * cosine + lower * sine], axis=-1)


def attend(query_matrix, key, value_matrix, slot_doc, slot_position_index):
    scale = query_matrix.shape[-1] ** -0.5
    scores = jnp.einsum("qgjd,kgd->gjqk", query_matrix.astype(jnp.float32), key.astype(jnp.float32)) * scale
    allowed = (slot_doc[:, None] == slot_doc[None, :]) & (slot_position_index[None, :] <= slot_position_index[:, None])
    scores = jnp.where(allowed[None, None], scores, -jnp.inf)
    peak = jnp.max(scores, axis=-1, keepdims=True)
    expo = jnp.exp(scores - peak)
    total = jnp.sum(expo, axis=-1)
    weights = expo.astype(jnp.bfloat16)
    mixed = jnp.einsum("gjqk,kgd->qgjd", weights.astype(jnp.float32), value_matrix.astype(jnp.float32))
    result = mixed / jnp.transpose(total, (2, 0, 1))[..., None]
    return result.astype(jnp.bfloat16)


def reference(tokens, wq, wk, wv, doc_len, doc_shard, doc_slot):
    source, filled, slot_doc, slot_position_index = slot_layout(doc_len, doc_shard, doc_slot, TOKENS, SHARD_SLOT_COUNT, SLOT_COUNT_ALL)
    joined = jnp.concatenate([wq, wk, wv], axis=1)
    width = MODEL_WIDTH // N_CTX
    summed = jnp.zeros((TOKENS, joined.shape[1]), jnp.float32)
    for block in range(N_CTX):
        term = jnp.dot(tokens[:, block * width:(block + 1) * width], joined[block * width:(block + 1) * width], preferred_element_type=jnp.float32).astype(jnp.bfloat16)
        summed = summed + term.astype(jnp.float32)
    projected = jnp.where(filled[:, None] == 1, jnp.take(summed, source, axis=0), jnp.float32(0.0))
    q_cols = QUERY_HEADS * HEAD_SIZE
    key_value_columns = KEY_VALUE_HEADS * HEAD_SIZE
    query_matrix = apply_rotary(projected[:, :q_cols].reshape(SLOT_COUNT_ALL, QUERY_HEADS, HEAD_SIZE), slot_position_index).astype(jnp.bfloat16)
    key_unrotated = lax.optimization_barrier(projected[:, q_cols:q_cols + key_value_columns].astype(jnp.bfloat16))
    value_matrix = projected[:, q_cols + key_value_columns:].astype(jnp.bfloat16)
    key = apply_rotary(key_unrotated.astype(jnp.float32).reshape(SLOT_COUNT_ALL, KEY_VALUE_HEADS, HEAD_SIZE), slot_position_index).astype(jnp.bfloat16)
    query_matrix = query_matrix.reshape(N_CTX, SHARD_SLOT_COUNT, KEY_VALUE_HEADS, QUERY_HEADS // KEY_VALUE_HEADS, HEAD_SIZE)
    key = key.reshape(N_CTX, SHARD_SLOT_COUNT, KEY_VALUE_HEADS, HEAD_SIZE)
    value_matrix = value_matrix.reshape(N_CTX, SHARD_SLOT_COUNT, KEY_VALUE_HEADS, HEAD_SIZE)
    docs = slot_doc.reshape(N_CTX, SHARD_SLOT_COUNT)
    places = slot_position_index.reshape(N_CTX, SHARD_SLOT_COUNT)
    outputs = lax.map(lambda items: attend(items[0], items[1], items[2], items[3], items[4]), (query_matrix, key, value_matrix, docs, places))
    return outputs.reshape(SLOT_COUNT_ALL, QUERY_HEADS * HEAD_SIZE)
```

```python
import jax
import jax.numpy as jnp
from jax import lax
from jax.sharding import PartitionSpec as P

HEAD_SIZE = 128


rope_base = 500000.0


def slot_table(slot_ids, doc_len, doc_shard, doc_slot, capacity):
    ends = jnp.cumsum(doc_len)
    starts = ends - doc_len
    shard_of = slot_ids // capacity
    local = slot_ids % capacity
    offset = local[:, None] - doc_slot[None, :]
    match = (
        (shard_of[:, None] == doc_shard[None, :]) & (offset >= 0) & (offset < doc_len[None, :])
    )
    filled = jnp.any(match, axis=1)
    position = jnp.sum(jnp.where(match, offset, 0), axis=1)
    source = jnp.sum(jnp.where(match, starts[None, :] + offset, 0), axis=1)
    doc_ids = jnp.arange(doc_len.shape[0], dtype=jnp.int32)
    doc_of = jnp.sum(jnp.where(match, doc_ids[None, :], 0), axis=1)
    slot_doc = jnp.where(filled, doc_of, -1 - slot_ids)
    return (source, filled, slot_doc, position)


def apply_rotary(values, positions):
    head_dim = values.shape[-1]
    half = head_dim // 2
    freq = jnp.power(
        jnp.float32(rope_base), -jnp.arange(half, dtype=jnp.float32) * (2.0 / head_dim)
    )
    angle = positions.astype(jnp.float32)[:, None] * freq[None, :]
    cosine = jnp.cos(angle)[:, None, :]
    sine = jnp.sin(angle)[:, None, :]
    lower = values[..., :half]
    upper = values[..., half:]
    return jnp.concatenate([lower * cosine - upper * sine, upper * cosine + lower * sine], axis=-1)


def attend(query_matrix, key, value_matrix, slot_doc, slot_position_index):
    scale = query_matrix.shape[-1] ** (-0.5)
    scores = (
        jnp.einsum("qgjd,kgd->gjqk", query_matrix, key, preferred_element_type=jnp.float32) * scale
    )
    allowed = (slot_doc[:, None] == slot_doc[None, :]) & (
        slot_position_index[None, :] <= slot_position_index[:, None]
    )
    scores = jnp.where(allowed[None, None], scores, -jnp.inf)
    peak = jnp.max(scores, axis=-1, keepdims=True)
    expo = jnp.exp(scores - peak)
    total = jnp.sum(expo, axis=-1)
    weights = expo.astype(jnp.bfloat16)
    mixed = jnp.einsum("gjqk,kgd->qgjd", weights, value_matrix, preferred_element_type=jnp.float32)
    result = mixed / jnp.transpose(total, (2, 0, 1))[..., None]
    return result.astype(jnp.bfloat16)


def body(tokens, wq, wk, wv, doc_len, doc_shard, doc_slot):
    shards = lax.axis_size("ctx")
    total_tokens = tokens.shape[0]
    per_shard = total_tokens // shards
    capacity = per_shard + per_shard // 2
    slot_total = capacity * shards
    q_cols = wq.shape[1]
    key_value_columns = wk.shape[1]
    members = HEAD_SIZE // key_value_columns
    groups = [
        list(range(g * members, (g + 1) * members))
        for g in range(lax.axis_size("tp") // members)
    ]
    pieces = lax.all_gather(
        jnp.concatenate([wk, wv], axis=1), "tp", axis=0, axis_index_groups=groups
    )
    width = pieces.shape[1]
    key_weights = jnp.transpose(pieces[:, :, :key_value_columns], (1, 0, 2)).reshape(width, HEAD_SIZE)
    value_weights = jnp.transpose(pieces[:, :, key_value_columns:], (1, 0, 2)).reshape(width, HEAD_SIZE)

    source, filled, _, _ = slot_table(
        jnp.arange(slot_total, dtype=jnp.int32), doc_len, doc_shard, doc_slot, capacity
    )
    token_ids = jnp.arange(total_tokens, dtype=jnp.int32)
    placement = ((source[:, None] == token_ids[None, :]) & filled[:, None]).astype(jnp.bfloat16)

    query_term = jnp.dot(tokens, wq, preferred_element_type=jnp.float32).astype(jnp.bfloat16)
    kv_term = jnp.dot(
        tokens, jnp.concatenate([key_weights, value_weights], axis=1), preferred_element_type=jnp.float32
    ).astype(jnp.bfloat16)
    term = jnp.concatenate([query_term, kv_term], axis=1)
    slot_rows = jnp.dot(placement, term, preferred_element_type=jnp.float32).astype(jnp.bfloat16)
    columns = slot_rows.shape[1]
    received = lax.all_to_all(
        slot_rows.reshape(shards, capacity, columns), "ctx", 0, 0, tiled=False
    )
    summed = jnp.sum(received.astype(jnp.float32), axis=0)

    shard = lax.axis_index("ctx")
    my_slots = shard * capacity + jnp.arange(capacity, dtype=jnp.int32)
    _, _, my_doc, my_pos = slot_table(my_slots, doc_len, doc_shard, doc_slot, capacity)
    heads_here = q_cols // HEAD_SIZE
    query_matrix = apply_rotary(
        summed[:, :q_cols].reshape(capacity, heads_here, HEAD_SIZE), my_pos
    ).astype(jnp.bfloat16)
    key_unrotated = lax.optimization_barrier(
        summed[:, q_cols : q_cols + HEAD_SIZE].astype(jnp.bfloat16)
    )
    value_matrix = summed[:, q_cols + HEAD_SIZE :].astype(jnp.bfloat16)
    key = apply_rotary(key_unrotated.astype(jnp.float32)[:, None, :], my_pos).astype(jnp.bfloat16)
    result = attend(
        query_matrix.reshape(capacity, 1, heads_here, HEAD_SIZE),
        key,
        value_matrix[:, None, :],
        my_doc,
        my_pos,
    )
    return result.reshape(capacity, heads_here * HEAD_SIZE)


def solution(mesh):
    return jax.shard_map(
        body,
        mesh=mesh,
        in_specs=(P(None, "ctx"), P("ctx", "tp"), P("ctx", "tp"), P("ctx", "tp"), P(), P(), P()),
        out_specs=P("ctx", "tp"),
        check_vma=False,
    )
```

```python
import jax
import jax.numpy as jnp
from jax import lax
from jax.sharding import PartitionSpec as P

HEAD_SIZE = 128


rope_base = 500000.0


def slot_table(slot_ids, doc_len, doc_shard, doc_slot, capacity):
    ends = jnp.cumsum(doc_len)
    starts = ends - doc_len
    shard_of = slot_ids // capacity
    local = slot_ids % capacity
    offset = local[:, None] - doc_slot[None, :]
    match = (
        (shard_of[:, None] == doc_shard[None, :]) & (offset >= 0) & (offset < doc_len[None, :])
    )
    filled = jnp.any(match, axis=1)
    position = jnp.sum(jnp.where(match, offset, 0), axis=1)
    source = jnp.sum(jnp.where(match, starts[None, :] + offset, 0), axis=1)
    doc_ids = jnp.arange(doc_len.shape[0], dtype=jnp.int32)
    doc_of = jnp.sum(jnp.where(match, doc_ids[None, :], 0), axis=1)
    slot_doc = jnp.where(filled, doc_of, -1 - slot_ids)
    return (source, filled, slot_doc, position)


def apply_rotary(values, positions):
    head_dim = values.shape[-1]
    half = head_dim // 2
    freq = jnp.power(
        jnp.float32(rope_base), -jnp.arange(half, dtype=jnp.float32) * (2.0 / head_dim)
    )
    angle = positions.astype(jnp.float32)[:, None] * freq[None, :]
    cosine = jnp.cos(angle)[:, None, :]
    sine = jnp.sin(angle)[:, None, :]
    lower = values[..., :half]
    upper = values[..., half:]
    return jnp.concatenate([lower * cosine - upper * sine, upper * cosine + lower * sine], axis=-1)


def attend(query_matrix, key, value_matrix, slot_doc, slot_position_index):
    scale = query_matrix.shape[-1] ** (-0.5)
    scores = (
        jnp.einsum("qgjd,kgd->gjqk", query_matrix, key, preferred_element_type=jnp.float32) * scale
    )
    allowed = (slot_doc[:, None] == slot_doc[None, :]) & (
        slot_position_index[None, :] <= slot_position_index[:, None]
    )
    scores = jnp.where(allowed[None, None], scores, -jnp.inf)
    peak = jnp.max(scores, axis=-1, keepdims=True)
    expo = jnp.exp(scores - peak)
    total = jnp.sum(expo, axis=-1)
    weights = expo.astype(jnp.bfloat16)
    mixed = jnp.einsum("gjqk,kgd->qgjd", weights, value_matrix, preferred_element_type=jnp.float32)
    result = mixed / jnp.transpose(total, (2, 0, 1))[..., None]
    return result.astype(jnp.bfloat16)


def body(tokens, wq, wk, wv, doc_len, doc_shard, doc_slot):
    shards = lax.axis_size("ctx")
    total_tokens = tokens.shape[0]
    per_shard = total_tokens // shards
    capacity = per_shard + per_shard // 2
    slot_total = capacity * shards
    q_cols = wq.shape[1]
    key_value_columns = wk.shape[1]
    members = HEAD_SIZE // key_value_columns
    groups = [
        list(range(g * members, (g + 1) * members))
        for g in range(lax.axis_size("tp") // members)
    ]

    source, filled, _, _ = slot_table(
        jnp.arange(slot_total, dtype=jnp.int32), doc_len, doc_shard, doc_slot, capacity
    )
    token_ids = jnp.arange(total_tokens, dtype=jnp.int32)
    placement = ((source[:, None] == token_ids[None, :]) & filled[:, None]).astype(jnp.bfloat16)

    joined = jnp.concatenate([wq, wk, wv], axis=1)
    term = jnp.dot(tokens, joined, preferred_element_type=jnp.float32).astype(jnp.bfloat16)
    slot_rows = jnp.dot(placement, term, preferred_element_type=jnp.float32).astype(jnp.bfloat16)
    columns = slot_rows.shape[1]
    received = lax.all_to_all(
        slot_rows.reshape(shards, capacity, columns), "ctx", 0, 0, tiled=False
    )
    summed = jnp.sum(received.astype(jnp.float32), axis=0)

    pieces = lax.all_gather(
        summed[:, q_cols:].astype(jnp.bfloat16), "tp", axis=0, axis_index_groups=groups
    )
    key_unrotated = jnp.transpose(pieces[:, :, :key_value_columns], (1, 0, 2)).reshape(capacity, HEAD_SIZE)
    value_matrix = jnp.transpose(pieces[:, :, key_value_columns:], (1, 0, 2)).reshape(capacity, HEAD_SIZE)

    shard = lax.axis_index("ctx")
    my_slots = shard * capacity + jnp.arange(capacity, dtype=jnp.int32)
    _, _, my_doc, my_pos = slot_table(my_slots, doc_len, doc_shard, doc_slot, capacity)
    heads_here = q_cols // HEAD_SIZE
    query_matrix = apply_rotary(
        summed[:, :q_cols].reshape(capacity, heads_here, HEAD_SIZE), my_pos
    ).astype(jnp.bfloat16)
    key = apply_rotary(key_unrotated.astype(jnp.float32)[:, None, :], my_pos).astype(jnp.bfloat16)
    result = attend(
        query_matrix.reshape(capacity, 1, heads_here, HEAD_SIZE),
        key,
        value_matrix[:, None, :],
        my_doc,
        my_pos,
    )
    return result.reshape(capacity, heads_here * HEAD_SIZE)


def solution(mesh):
    return jax.shard_map(
        body,
        mesh=mesh,
        in_specs=(P(None, "ctx"), P("ctx", "tp"), P("ctx", "tp"), P("ctx", "tp"), P(), P(), P()),
        out_specs=P("ctx", "tp"),
        check_vma=False,
    )
```

```python
import jax
import jax.numpy as jnp
from jax import lax
from jax.sharding import PartitionSpec as P

HEAD_SIZE = 128


rope_base = 500000.0


def slot_table(slot_ids, doc_len, doc_shard, doc_slot, capacity):
    ends = jnp.cumsum(doc_len)
    starts = ends - doc_len
    shard_of = slot_ids // capacity
    local = slot_ids % capacity
    offset = local[:, None] - doc_slot[None, :]
    match = (
        (shard_of[:, None] == doc_shard[None, :]) & (offset >= 0) & (offset < doc_len[None, :])
    )
    filled = jnp.any(match, axis=1)
    position = jnp.sum(jnp.where(match, offset, 0), axis=1)
    source = jnp.sum(jnp.where(match, starts[None, :] + offset, 0), axis=1)
    doc_ids = jnp.arange(doc_len.shape[0], dtype=jnp.int32)
    doc_of = jnp.sum(jnp.where(match, doc_ids[None, :], 0), axis=1)
    slot_doc = jnp.where(filled, doc_of, -1 - slot_ids)
    return (source, filled, slot_doc, position)


def apply_rotary(values, positions):
    head_dim = values.shape[-1]
    half = head_dim // 2
    freq = jnp.power(
        jnp.float32(rope_base), -jnp.arange(half, dtype=jnp.float32) * (2.0 / head_dim)
    )
    angle = positions.astype(jnp.float32)[:, None] * freq[None, :]
    cosine = jnp.cos(angle)[:, None, :]
    sine = jnp.sin(angle)[:, None, :]
    lower = values[..., :half]
    upper = values[..., half:]
    return jnp.concatenate([lower * cosine - upper * sine, upper * cosine + lower * sine], axis=-1)


def attend(query_matrix, key, value_matrix, slot_doc, slot_position_index):
    scale = query_matrix.shape[-1] ** (-0.5)
    scores = (
        jnp.einsum("qgjd,kgd->gjqk", query_matrix, key, preferred_element_type=jnp.float32) * scale
    )
    allowed = (slot_doc[:, None] == slot_doc[None, :]) & (
        slot_position_index[None, :] <= slot_position_index[:, None]
    )
    scores = jnp.where(allowed[None, None], scores, -jnp.inf)
    peak = jnp.max(scores, axis=-1, keepdims=True)
    expo = jnp.exp(scores - peak)
    total = jnp.sum(expo, axis=-1)
    weights = expo.astype(jnp.bfloat16)
    mixed = jnp.einsum("gjqk,kgd->qgjd", weights, value_matrix, preferred_element_type=jnp.float32)
    result = mixed / jnp.transpose(total, (2, 0, 1))[..., None]
    return result.astype(jnp.bfloat16)


def body(tokens, wq, wk, wv, doc_len, doc_shard, doc_slot):
    shards = lax.axis_size("ctx")
    total_tokens = tokens.shape[0]
    per_shard = total_tokens // shards
    capacity = per_shard + per_shard // 2
    slot_total = capacity * shards
    q_cols = wq.shape[1]
    key_value_columns = wk.shape[1]
    members = HEAD_SIZE // key_value_columns
    groups = [
        list(range(g * members, (g + 1) * members))
        for g in range(lax.axis_size("tp") // members)
    ]

    source, filled, _, _ = slot_table(
        jnp.arange(slot_total, dtype=jnp.int32), doc_len, doc_shard, doc_slot, capacity
    )
    token_ids = jnp.arange(total_tokens, dtype=jnp.int32)
    placement = ((source[:, None] == token_ids[None, :]) & filled[:, None]).astype(jnp.bfloat16)

    joined = jnp.concatenate([wq, wk, wv], axis=1)
    term = jnp.dot(tokens, joined, preferred_element_type=jnp.float32).astype(jnp.bfloat16)
    slot_rows = jnp.einsum(
        "jf,csj->cfs",
        term,
        placement.reshape(shards, capacity, total_tokens),
        preferred_element_type=jnp.float32,
    ).astype(jnp.bfloat16)
    received = lax.all_to_all(slot_rows, "ctx", 0, 0, tiled=False)
    summed = jnp.transpose(jnp.sum(received.astype(jnp.float32), axis=0))

    pieces = lax.all_gather(
        summed[:, q_cols:].astype(jnp.bfloat16), "tp", axis=0, axis_index_groups=groups
    )
    key_unrotated = jnp.transpose(pieces[:, :, :key_value_columns], (1, 0, 2)).reshape(capacity, HEAD_SIZE)
    value_matrix = jnp.transpose(pieces[:, :, key_value_columns:], (1, 0, 2)).reshape(capacity, HEAD_SIZE)

    shard = lax.axis_index("ctx")
    my_slots = shard * capacity + jnp.arange(capacity, dtype=jnp.int32)
    _, _, my_doc, my_pos = slot_table(my_slots, doc_len, doc_shard, doc_slot, capacity)
    heads_here = q_cols // HEAD_SIZE
    query_matrix = apply_rotary(
        summed[:, :q_cols].reshape(capacity, heads_here, HEAD_SIZE), my_pos
    ).astype(jnp.bfloat16)
    key = apply_rotary(key_unrotated.astype(jnp.float32)[:, None, :], my_pos).astype(jnp.bfloat16)
    result = attend(
        query_matrix.reshape(capacity, 1, heads_here, HEAD_SIZE),
        key,
        value_matrix[:, None, :],
        my_doc,
        my_pos,
    )
    return result.reshape(capacity, heads_here * HEAD_SIZE)


def solution(mesh):
    return jax.shard_map(
        body,
        mesh=mesh,
        in_specs=(P(None, "ctx"), P("ctx", "tp"), P("ctx", "tp"), P("ctx", "tp"), P(), P(), P()),
        out_specs=P("ctx", "tp"),
        check_vma=False,
    )
```

```python
import jax
import jax.numpy as jnp
from jax import lax
from jax.sharding import PartitionSpec as P

HEAD_SIZE = 128


rope_base = 500000.0


def slot_table(slot_ids, doc_len, doc_shard, doc_slot, capacity):
    ends = jnp.cumsum(doc_len)
    starts = ends - doc_len
    shard_of = slot_ids // capacity
    local = slot_ids % capacity
    offset = local[:, None] - doc_slot[None, :]
    match = (
        (shard_of[:, None] == doc_shard[None, :]) & (offset >= 0) & (offset < doc_len[None, :])
    )
    filled = jnp.any(match, axis=1)
    position = jnp.sum(jnp.where(match, offset, 0), axis=1)
    source = jnp.sum(jnp.where(match, starts[None, :] + offset, 0), axis=1)
    doc_ids = jnp.arange(doc_len.shape[0], dtype=jnp.int32)
    doc_of = jnp.sum(jnp.where(match, doc_ids[None, :], 0), axis=1)
    slot_doc = jnp.where(filled, doc_of, -1 - slot_ids)
    return (source, filled, slot_doc, position)


def apply_rotary(values, positions):
    head_dim = values.shape[-1]
    half = head_dim // 2
    freq = jnp.power(
        jnp.float32(rope_base), -jnp.arange(half, dtype=jnp.float32) * (2.0 / head_dim)
    )
    angle = positions.astype(jnp.float32)[:, None] * freq[None, :]
    cosine = jnp.cos(angle)[:, None, :]
    sine = jnp.sin(angle)[:, None, :]
    lower = values[..., :half]
    upper = values[..., half:]
    return jnp.concatenate([lower * cosine - upper * sine, upper * cosine + lower * sine], axis=-1)


def attend(query_matrix, key, value_matrix, slot_doc, slot_position_index):
    scale = query_matrix.shape[-1] ** (-0.5)
    scores = (
        jnp.einsum("qgjd,kgd->gjqk", query_matrix, key, preferred_element_type=jnp.float32) * scale
    )
    allowed = (slot_doc[:, None] == slot_doc[None, :]) & (
        slot_position_index[None, :] <= slot_position_index[:, None]
    )
    scores = jnp.where(allowed[None, None], scores, -jnp.inf)
    peak = jnp.max(scores, axis=-1, keepdims=True)
    expo = jnp.exp(scores - peak)
    total = jnp.sum(expo, axis=-1)
    weights = expo.astype(jnp.bfloat16)
    mixed = jnp.einsum("gjqk,kgd->qgjd", weights, value_matrix, preferred_element_type=jnp.float32)
    result = mixed / jnp.transpose(total, (2, 0, 1))[..., None]
    return result.astype(jnp.bfloat16)


def body(tokens, wq, wk, wv, doc_len, doc_shard, doc_slot):
    shards = lax.axis_size("ctx")
    total_tokens = tokens.shape[0]
    per_shard = total_tokens // shards
    capacity = per_shard + per_shard // 2
    slot_total = capacity * shards
    q_cols = wq.shape[1]
    key_value_columns = wk.shape[1]
    members = HEAD_SIZE // key_value_columns
    groups = [
        list(range(g * members, (g + 1) * members))
        for g in range(lax.axis_size("tp") // members)
    ]

    source, filled, _, _ = slot_table(
        jnp.arange(slot_total, dtype=jnp.int32), doc_len, doc_shard, doc_slot, capacity
    )
    token_ids = jnp.arange(total_tokens, dtype=jnp.int32)
    placement = ((source[:, None] == token_ids[None, :]) & filled[:, None]).astype(jnp.bfloat16)

    joined = jnp.concatenate([wq, wk, wv], axis=1)
    term = jnp.dot(tokens, joined, preferred_element_type=jnp.float32).astype(jnp.bfloat16)
    slot_rows = jnp.einsum(
        "jf,csj->cfs",
        term,
        placement.reshape(shards, capacity, total_tokens),
        preferred_element_type=jnp.float32,
    ).astype(jnp.bfloat16)
    kv_received = lax.all_to_all(slot_rows[:, q_cols:], "ctx", 0, 0, tiled=False)
    kv_summed = lax.optimization_barrier(jnp.sum(kv_received.astype(jnp.float32), axis=0))
    pieces = lax.all_gather(
        jnp.transpose(kv_summed).astype(jnp.bfloat16), "tp", axis=0, axis_index_groups=groups
    )
    q_received = lax.all_to_all(slot_rows[:, :q_cols], "ctx", 0, 0, tiled=False)
    q_summed = jnp.transpose(jnp.sum(q_received.astype(jnp.float32), axis=0))
    key_unrotated = jnp.transpose(pieces[:, :, :key_value_columns], (1, 0, 2)).reshape(capacity, HEAD_SIZE)
    value_matrix = jnp.transpose(pieces[:, :, key_value_columns:], (1, 0, 2)).reshape(capacity, HEAD_SIZE)

    shard = lax.axis_index("ctx")
    my_slots = shard * capacity + jnp.arange(capacity, dtype=jnp.int32)
    _, _, my_doc, my_pos = slot_table(my_slots, doc_len, doc_shard, doc_slot, capacity)
    heads_here = q_cols // HEAD_SIZE
    query_matrix = apply_rotary(
        q_summed.reshape(capacity, heads_here, HEAD_SIZE), my_pos
    ).astype(jnp.bfloat16)
    key = apply_rotary(key_unrotated.astype(jnp.float32)[:, None, :], my_pos).astype(jnp.bfloat16)
    result = attend(
        query_matrix.reshape(capacity, 1, heads_here, HEAD_SIZE),
        key,
        value_matrix[:, None, :],
        my_doc,
        my_pos,
    )
    return result.reshape(capacity, heads_here * HEAD_SIZE)


def solution(mesh):
    return jax.shard_map(
        body,
        mesh=mesh,
        in_specs=(P(None, "ctx"), P("ctx", "tp"), P("ctx", "tp"), P("ctx", "tp"), P(), P(), P()),
        out_specs=P("ctx", "tp"),
        check_vma=False,
    )
```

```python
import jax
import jax.numpy as jnp
from jax import lax
from jax.sharding import PartitionSpec as P

HEAD_SIZE = 128


rope_base = 500000.0


def slot_table(slot_ids, doc_len, doc_shard, doc_slot, capacity):
    ends = jnp.cumsum(doc_len)
    starts = ends - doc_len
    shard_of = slot_ids // capacity
    local = slot_ids % capacity
    offset = local[:, None] - doc_slot[None, :]
    match = (
        (shard_of[:, None] == doc_shard[None, :]) & (offset >= 0) & (offset < doc_len[None, :])
    )
    filled = jnp.any(match, axis=1)
    position = jnp.sum(jnp.where(match, offset, 0), axis=1)
    source = jnp.sum(jnp.where(match, starts[None, :] + offset, 0), axis=1)
    doc_ids = jnp.arange(doc_len.shape[0], dtype=jnp.int32)
    doc_of = jnp.sum(jnp.where(match, doc_ids[None, :], 0), axis=1)
    slot_doc = jnp.where(filled, doc_of, -1 - slot_ids)
    return (source, filled, slot_doc, position)


def apply_rotary(values, positions):
    head_dim = values.shape[-1]
    half = head_dim // 2
    freq = jnp.power(
        jnp.float32(rope_base), -jnp.arange(half, dtype=jnp.float32) * (2.0 / head_dim)
    )
    angle = positions.astype(jnp.float32)[:, None] * freq[None, :]
    cosine = jnp.cos(angle)[:, None, :]
    sine = jnp.sin(angle)[:, None, :]
    lower = values[..., :half]
    upper = values[..., half:]
    return jnp.concatenate([lower * cosine - upper * sine, upper * cosine + lower * sine], axis=-1)


def attend(query_matrix, key, value_matrix, slot_doc, slot_position_index):
    scale = query_matrix.shape[-1] ** (-0.5)
    scores = (
        jnp.einsum("qgjd,kgd->gjqk", query_matrix, key, preferred_element_type=jnp.float32) * scale
    )
    allowed = (slot_doc[:, None] == slot_doc[None, :]) & (
        slot_position_index[None, :] <= slot_position_index[:, None]
    )
    scores = jnp.where(allowed[None, None], scores, -jnp.inf)
    peak = jnp.max(scores, axis=-1, keepdims=True)
    expo = jnp.exp(scores - peak)
    total = jnp.sum(expo, axis=-1)
    weights = expo.astype(jnp.bfloat16)
    mixed = jnp.einsum("gjqk,kgd->qgjd", weights, value_matrix, preferred_element_type=jnp.float32)
    result = mixed / jnp.transpose(total, (2, 0, 1))[..., None]
    return result.astype(jnp.bfloat16)


def body(tokens, wq, wk, wv, doc_len, doc_shard, doc_slot):
    shards = lax.axis_size("ctx")
    total_tokens = tokens.shape[0]
    per_shard = total_tokens // shards
    capacity = per_shard + per_shard // 2
    slot_total = capacity * shards
    q_cols = wq.shape[1]
    key_value_columns = wk.shape[1]
    members = HEAD_SIZE // key_value_columns
    groups = [
        list(range(g * members, (g + 1) * members))
        for g in range(lax.axis_size("tp") // members)
    ]

    source, filled, _, _ = slot_table(
        jnp.arange(slot_total, dtype=jnp.int32), doc_len, doc_shard, doc_slot, capacity
    )
    token_ids = jnp.arange(total_tokens, dtype=jnp.int32)
    placement = ((source[:, None] == token_ids[None, :]) & filled[:, None]).astype(jnp.bfloat16)

    def placed(weights):
        term = jnp.dot(tokens, weights, preferred_element_type=jnp.float32).astype(jnp.bfloat16)
        return jnp.einsum(
            "jf,csj->cfs",
            term,
            placement.reshape(shards, capacity, total_tokens),
            preferred_element_type=jnp.float32,
        ).astype(jnp.bfloat16)

    kv_received = lax.all_to_all(placed(jnp.concatenate([wk, wv], axis=1)), "ctx", 0, 0, tiled=False)
    q_received = lax.all_to_all(placed(wq), "ctx", 0, 0, tiled=False)
    kv_summed = lax.optimization_barrier(jnp.sum(kv_received.astype(jnp.float32), axis=0))
    pieces = lax.all_gather(
        jnp.transpose(kv_summed).astype(jnp.bfloat16), "tp", axis=0, axis_index_groups=groups
    )
    q_summed = jnp.transpose(jnp.sum(q_received.astype(jnp.float32), axis=0))
    key_unrotated = jnp.transpose(pieces[:, :, :key_value_columns], (1, 0, 2)).reshape(capacity, HEAD_SIZE)
    value_matrix = jnp.transpose(pieces[:, :, key_value_columns:], (1, 0, 2)).reshape(capacity, HEAD_SIZE)

    shard = lax.axis_index("ctx")
    my_slots = shard * capacity + jnp.arange(capacity, dtype=jnp.int32)
    _, _, my_doc, my_pos = slot_table(my_slots, doc_len, doc_shard, doc_slot, capacity)
    heads_here = q_cols // HEAD_SIZE
    query_matrix = apply_rotary(
        q_summed.reshape(capacity, heads_here, HEAD_SIZE), my_pos
    ).astype(jnp.bfloat16)
    key = apply_rotary(key_unrotated.astype(jnp.float32)[:, None, :], my_pos).astype(jnp.bfloat16)
    result = attend(
        query_matrix.reshape(capacity, 1, heads_here, HEAD_SIZE),
        key,
        value_matrix[:, None, :],
        my_doc,
        my_pos,
    )
    return result.reshape(capacity, heads_here * HEAD_SIZE)


def solution(mesh):
    return jax.shard_map(
        body,
        mesh=mesh,
        in_specs=(P(None, "ctx"), P("ctx", "tp"), P("ctx", "tp"), P("ctx", "tp"), P(), P(), P()),
        out_specs=P("ctx", "tp"),
        check_vma=False,
    )
```

```python
import jax
import jax.numpy as jnp
from jax import lax
from jax.sharding import PartitionSpec as P

HEAD_SIZE = 128


rope_base = 500000.0


def slot_table(slot_ids, doc_len, doc_shard, doc_slot, capacity):
    ends = jnp.cumsum(doc_len)
    starts = ends - doc_len
    shard_of = slot_ids // capacity
    local = slot_ids % capacity
    offset = local[:, None] - doc_slot[None, :]
    match = (
        (shard_of[:, None] == doc_shard[None, :]) & (offset >= 0) & (offset < doc_len[None, :])
    )
    filled = jnp.any(match, axis=1)
    position = jnp.sum(jnp.where(match, offset, 0), axis=1)
    source = jnp.sum(jnp.where(match, starts[None, :] + offset, 0), axis=1)
    doc_ids = jnp.arange(doc_len.shape[0], dtype=jnp.int32)
    doc_of = jnp.sum(jnp.where(match, doc_ids[None, :], 0), axis=1)
    slot_doc = jnp.where(filled, doc_of, -1 - slot_ids)
    return (source, filled, slot_doc, position)


def apply_rotary(values, positions):
    head_dim = values.shape[-1]
    half = head_dim // 2
    freq = jnp.power(
        jnp.float32(rope_base), -jnp.arange(half, dtype=jnp.float32) * (2.0 / head_dim)
    )
    angle = positions.astype(jnp.float32)[:, None] * freq[None, :]
    cosine = jnp.cos(angle)[:, None, :]
    sine = jnp.sin(angle)[:, None, :]
    lower = values[..., :half]
    upper = values[..., half:]
    return jnp.concatenate([lower * cosine - upper * sine, upper * cosine + lower * sine], axis=-1)


def attend(query_matrix, key, value_matrix, slot_doc, slot_position_index):
    scale = query_matrix.shape[-1] ** (-0.5)
    scores = (
        jnp.einsum("qgjd,kgd->gjqk", query_matrix, key, preferred_element_type=jnp.float32) * scale
    )
    allowed = (slot_doc[:, None] == slot_doc[None, :]) & (
        slot_position_index[None, :] <= slot_position_index[:, None]
    )
    scores = jnp.where(allowed[None, None], scores, -jnp.inf)
    peak = jnp.max(scores, axis=-1, keepdims=True)
    expo = jnp.exp(scores - peak)
    total = jnp.sum(expo, axis=-1)
    weights = expo.astype(jnp.bfloat16)
    mixed = jnp.einsum("gjqk,kgd->qgjd", weights, value_matrix, preferred_element_type=jnp.float32)
    result = mixed / jnp.transpose(total, (2, 0, 1))[..., None]
    return result.astype(jnp.bfloat16)


def body(tokens, wq, wk, wv, doc_len, doc_shard, doc_slot):
    shards = lax.axis_size("ctx")
    total_tokens = tokens.shape[0]
    per_shard = total_tokens // shards
    capacity = per_shard + per_shard // 2
    slot_total = capacity * shards
    q_cols = wq.shape[1]
    key_value_columns = wk.shape[1]
    members = HEAD_SIZE // key_value_columns
    groups = [
        list(range(g * members, (g + 1) * members))
        for g in range(lax.axis_size("tp") // members)
    ]

    source, filled, _, _ = slot_table(
        jnp.arange(slot_total, dtype=jnp.int32), doc_len, doc_shard, doc_slot, capacity
    )
    token_ids = jnp.arange(total_tokens, dtype=jnp.int32)
    placement = ((source[:, None] == token_ids[None, :]) & filled[:, None]).astype(jnp.bfloat16)

    def placed(weights):
        term = lax.optimization_barrier(
            jnp.dot(tokens, weights, preferred_element_type=jnp.float32).astype(jnp.bfloat16)
        )
        return jnp.einsum(
            "jf,csj->cfs",
            term,
            placement.reshape(shards, capacity, total_tokens),
            preferred_element_type=jnp.float32,
        ).astype(jnp.bfloat16)

    kv_received = lax.all_to_all(placed(jnp.concatenate([wk, wv], axis=1)), "ctx", 0, 0, tiled=False)
    q_received = lax.all_to_all(placed(wq), "ctx", 0, 0, tiled=False)
    kv_summed = lax.optimization_barrier(jnp.sum(kv_received.astype(jnp.float32), axis=0))
    pieces = lax.all_gather(
        jnp.transpose(kv_summed).astype(jnp.bfloat16), "tp", axis=0, axis_index_groups=groups
    )
    q_summed = jnp.transpose(jnp.sum(q_received.astype(jnp.float32), axis=0))
    key_unrotated = jnp.transpose(pieces[:, :, :key_value_columns], (1, 0, 2)).reshape(capacity, HEAD_SIZE)
    value_matrix = jnp.transpose(pieces[:, :, key_value_columns:], (1, 0, 2)).reshape(capacity, HEAD_SIZE)

    shard = lax.axis_index("ctx")
    my_slots = shard * capacity + jnp.arange(capacity, dtype=jnp.int32)
    _, _, my_doc, my_pos = slot_table(my_slots, doc_len, doc_shard, doc_slot, capacity)
    heads_here = q_cols // HEAD_SIZE
    query_matrix = apply_rotary(
        q_summed.reshape(capacity, heads_here, HEAD_SIZE), my_pos
    ).astype(jnp.bfloat16)
    key = apply_rotary(key_unrotated.astype(jnp.float32)[:, None, :], my_pos).astype(jnp.bfloat16)
    result = attend(
        query_matrix.reshape(capacity, 1, heads_here, HEAD_SIZE),
        key,
        value_matrix[:, None, :],
        my_doc,
        my_pos,
    )
    return result.reshape(capacity, heads_here * HEAD_SIZE)


def solution(mesh):
    return jax.shard_map(
        body,
        mesh=mesh,
        in_specs=(P(None, "ctx"), P("ctx", "tp"), P("ctx", "tp"), P("ctx", "tp"), P(), P(), P()),
        out_specs=P("ctx", "tp"),
        check_vma=False,
    )
```

```python
import jax
import jax.numpy as jnp
from jax import lax
from jax.sharding import PartitionSpec as P

HEAD_SIZE = 128


rope_base = 500000.0


def slot_table(slot_ids, doc_len, doc_shard, doc_slot, capacity):
    doc_ids = jnp.arange(doc_len.shape[0], dtype=jnp.int32)
    starts = jnp.sum(jnp.where(doc_ids[None, :] < doc_ids[:, None], doc_len[None, :], 0), axis=1)
    shard_of = slot_ids // capacity
    local = slot_ids % capacity
    offset = local[:, None] - doc_slot[None, :]
    match = (
        (shard_of[:, None] == doc_shard[None, :]) & (offset >= 0) & (offset < doc_len[None, :])
    )
    filled = jnp.any(match, axis=1)
    position = jnp.sum(jnp.where(match, offset, 0), axis=1)
    source = jnp.sum(jnp.where(match, starts[None, :] + offset, 0), axis=1)
    doc_of = jnp.sum(jnp.where(match, doc_ids[None, :], 0), axis=1)
    slot_doc = jnp.where(filled, doc_of, -1 - slot_ids)
    return (source, filled, slot_doc, position)


def apply_rotary(values, positions):
    head_dim = values.shape[-1]
    half = head_dim // 2
    freq = jnp.power(
        jnp.float32(rope_base), -jnp.arange(half, dtype=jnp.float32) * (2.0 / head_dim)
    )
    angle = positions.astype(jnp.float32)[:, None] * freq[None, :]
    cosine = jnp.cos(angle)[:, None, :]
    sine = jnp.sin(angle)[:, None, :]
    lower = values[..., :half]
    upper = values[..., half:]
    return jnp.concatenate([lower * cosine - upper * sine, upper * cosine + lower * sine], axis=-1)


def attend(query_matrix, key, value_matrix, slot_doc, slot_position_index):
    scale = query_matrix.shape[-1] ** (-0.5)
    scores = (
        jnp.einsum("qgjd,kgd->gjqk", query_matrix, key, preferred_element_type=jnp.float32) * scale
    )
    allowed = (slot_doc[:, None] == slot_doc[None, :]) & (
        slot_position_index[None, :] <= slot_position_index[:, None]
    )
    scores = jnp.where(allowed[None, None], scores, -jnp.inf)
    peak = jnp.max(scores, axis=-1, keepdims=True)
    expo = jnp.exp(scores - peak)
    total = jnp.sum(expo, axis=-1)
    weights = expo.astype(jnp.bfloat16)
    mixed = jnp.einsum("gjqk,kgd->qgjd", weights, value_matrix, preferred_element_type=jnp.float32)
    result = mixed / jnp.transpose(total, (2, 0, 1))[..., None]
    return result.astype(jnp.bfloat16)


def body(tokens, wq, wk, wv, doc_len, doc_shard, doc_slot):
    shards = lax.axis_size("ctx")
    total_tokens = tokens.shape[0]
    per_shard = total_tokens // shards
    capacity = per_shard + per_shard // 2
    slot_total = capacity * shards
    q_cols = wq.shape[1]
    key_value_columns = wk.shape[1]
    members = HEAD_SIZE // key_value_columns
    groups = [
        list(range(g * members, (g + 1) * members))
        for g in range(lax.axis_size("tp") // members)
    ]

    source, filled, _, _ = slot_table(
        jnp.arange(slot_total, dtype=jnp.int32), doc_len, doc_shard, doc_slot, capacity
    )
    token_ids = jnp.arange(total_tokens, dtype=jnp.int32)
    source = jnp.where(filled, source, -1)
    placement = (source[:, None] == token_ids[None, :]).astype(jnp.bfloat16)

    def placed(weights):
        term = lax.optimization_barrier(
            jnp.dot(tokens, weights, preferred_element_type=jnp.float32).astype(jnp.bfloat16)
        )
        return jnp.einsum(
            "jf,csj->cfs",
            term,
            placement.reshape(shards, capacity, total_tokens),
            preferred_element_type=jnp.float32,
        ).astype(jnp.bfloat16)

    kv_received = lax.all_to_all(placed(jnp.concatenate([wk, wv], axis=1)), "ctx", 0, 0, tiled=False)
    q_received = lax.all_to_all(placed(wq), "ctx", 0, 0, tiled=False)
    kv_summed = lax.optimization_barrier(jnp.sum(kv_received.astype(jnp.float32), axis=0))
    pieces = lax.all_gather(
        jnp.transpose(kv_summed).astype(jnp.bfloat16), "tp", axis=0, axis_index_groups=groups
    )
    q_summed = jnp.transpose(jnp.sum(q_received.astype(jnp.float32), axis=0))
    key_unrotated = jnp.transpose(pieces[:, :, :key_value_columns], (1, 0, 2)).reshape(capacity, HEAD_SIZE)
    value_matrix = jnp.transpose(pieces[:, :, key_value_columns:], (1, 0, 2)).reshape(capacity, HEAD_SIZE)

    shard = lax.axis_index("ctx")
    my_slots = shard * capacity + jnp.arange(capacity, dtype=jnp.int32)
    _, _, my_doc, my_pos = slot_table(my_slots, doc_len, doc_shard, doc_slot, capacity)
    heads_here = q_cols // HEAD_SIZE
    query_matrix = apply_rotary(
        q_summed.reshape(capacity, heads_here, HEAD_SIZE), my_pos
    ).astype(jnp.bfloat16)
    key = apply_rotary(key_unrotated.astype(jnp.float32)[:, None, :], my_pos).astype(jnp.bfloat16)
    result = attend(
        query_matrix.reshape(capacity, 1, heads_here, HEAD_SIZE),
        key,
        value_matrix[:, None, :],
        my_doc,
        my_pos,
    )
    return result.reshape(capacity, heads_here * HEAD_SIZE)


def solution(mesh):
    return jax.shard_map(
        body,
        mesh=mesh,
        in_specs=(P(None, "ctx"), P("ctx", "tp"), P("ctx", "tp"), P("ctx", "tp"), P(), P(), P()),
        out_specs=P("ctx", "tp"),
        check_vma=False,
    )
```

```python
import jax
import jax.numpy as jnp
from jax import lax
from jax.sharding import PartitionSpec as P

HEAD_SIZE = 128


rope_base = 500000.0


def slot_table(slot_ids, doc_len, doc_shard, doc_slot, capacity):
    doc_ids = jnp.arange(doc_len.shape[0], dtype=jnp.int32)
    starts = jnp.sum(jnp.where(doc_ids[None, :] < doc_ids[:, None], doc_len[None, :], 0), axis=1)
    shard_of = slot_ids // capacity
    local = slot_ids % capacity
    offset = local[:, None] - doc_slot[None, :]
    match = (
        (shard_of[:, None] == doc_shard[None, :]) & (offset >= 0) & (offset < doc_len[None, :])
    )
    filled = jnp.any(match, axis=1)
    position = jnp.sum(jnp.where(match, offset, 0), axis=1)
    source = jnp.sum(jnp.where(match, starts[None, :] + offset, 0), axis=1)
    doc_of = jnp.sum(jnp.where(match, doc_ids[None, :], 0), axis=1)
    slot_doc = jnp.where(filled, doc_of, -1 - slot_ids)
    return (source, filled, slot_doc, position)


def apply_rotary(values, positions):
    head_dim = values.shape[-1]
    half = head_dim // 2
    freq = jnp.power(
        jnp.float32(rope_base), -jnp.arange(half, dtype=jnp.float32) * (2.0 / head_dim)
    )
    angle = positions.astype(jnp.float32)[:, None] * freq[None, :]
    cosine = jnp.cos(angle)[:, None, :]
    sine = jnp.sin(angle)[:, None, :]
    lower = values[..., :half]
    upper = values[..., half:]
    return jnp.concatenate([lower * cosine - upper * sine, upper * cosine + lower * sine], axis=-1)


def attend(query_matrix, key, value_matrix, slot_doc, slot_position_index):
    scale = query_matrix.shape[-1] ** (-0.5)
    scores = (
        jnp.einsum("qgjd,kgd->gjqk", query_matrix, key, preferred_element_type=jnp.float32) * scale
    )
    allowed = (slot_doc[:, None] == slot_doc[None, :]) & (
        slot_position_index[None, :] <= slot_position_index[:, None]
    )
    scores = jnp.where(allowed[None, None], scores, -jnp.inf)
    peak = jnp.max(scores, axis=-1, keepdims=True)
    expo = jnp.exp(scores - peak)
    total = jnp.sum(expo, axis=-1)
    weights = expo.astype(jnp.bfloat16)
    mixed = jnp.einsum("gjqk,kgd->qgjd", weights, value_matrix, preferred_element_type=jnp.float32)
    result = mixed / jnp.transpose(total, (2, 0, 1))[..., None]
    return result.astype(jnp.bfloat16)


def body(tokens, wq, wk, wv, doc_len, doc_shard, doc_slot):
    shards = lax.axis_size("ctx")
    total_tokens = tokens.shape[0]
    per_shard = total_tokens // shards
    capacity = per_shard + per_shard // 2
    slot_total = capacity * shards
    q_cols = wq.shape[1]
    key_value_columns = wk.shape[1]
    members = HEAD_SIZE // key_value_columns
    groups = [
        list(range(g * members, (g + 1) * members))
        for g in range(lax.axis_size("tp") // members)
    ]

    source, filled, _, _ = slot_table(
        jnp.arange(slot_total, dtype=jnp.int32), doc_len, doc_shard, doc_slot, capacity
    )
    token_ids = jnp.arange(total_tokens, dtype=jnp.int32)
    source = jnp.where(filled, source, -1)
    placement = (source[:, None] == token_ids[None, :]).astype(jnp.bfloat16)

    def placed(weights):
        term = lax.optimization_barrier(
            jnp.dot(tokens, weights, preferred_element_type=jnp.float32).astype(jnp.bfloat16)
        )
        return jnp.einsum(
            "jf,csj->cfs",
            term,
            placement.reshape(shards, capacity, total_tokens),
            preferred_element_type=jnp.float32,
        ).astype(jnp.bfloat16)

    kv_term = jnp.dot(
        tokens, jnp.concatenate([wk, wv], axis=1), preferred_element_type=jnp.float32
    ).astype(jnp.bfloat16)
    kv_full = lax.psum(kv_term, "ctx")
    q_received = lax.all_to_all(placed(wq), "ctx", 0, 0, tiled=False)
    shard = lax.axis_index("ctx")
    my_source = lax.dynamic_slice_in_dim(source, shard * capacity, capacity)
    mine = (my_source[:, None] == token_ids[None, :]).astype(jnp.bfloat16)
    kv_mine = jnp.dot(mine, kv_full, preferred_element_type=jnp.float32).astype(jnp.bfloat16)
    pieces = lax.all_gather(kv_mine, "tp", axis=0, axis_index_groups=groups)
    q_summed = jnp.transpose(jnp.sum(q_received.astype(jnp.float32), axis=0))
    key_unrotated = jnp.transpose(pieces[:, :, :key_value_columns], (1, 0, 2)).reshape(capacity, HEAD_SIZE)
    value_matrix = jnp.transpose(pieces[:, :, key_value_columns:], (1, 0, 2)).reshape(capacity, HEAD_SIZE)

    my_slots = shard * capacity + jnp.arange(capacity, dtype=jnp.int32)
    _, _, my_doc, my_pos = slot_table(my_slots, doc_len, doc_shard, doc_slot, capacity)
    heads_here = q_cols // HEAD_SIZE
    query_matrix = apply_rotary(
        q_summed.reshape(capacity, heads_here, HEAD_SIZE), my_pos
    ).astype(jnp.bfloat16)
    key = apply_rotary(key_unrotated.astype(jnp.float32)[:, None, :], my_pos).astype(jnp.bfloat16)
    result = attend(
        query_matrix.reshape(capacity, 1, heads_here, HEAD_SIZE),
        key,
        value_matrix[:, None, :],
        my_doc,
        my_pos,
    )
    return result.reshape(capacity, heads_here * HEAD_SIZE)


def solution(mesh):
    return jax.shard_map(
        body,
        mesh=mesh,
        in_specs=(P(None, "ctx"), P("ctx", "tp"), P("ctx", "tp"), P("ctx", "tp"), P(), P(), P()),
        out_specs=P("ctx", "tp"),
        check_vma=False,
    )
```

```python
import jax
import jax.numpy as jnp
from jax import lax
from jax.sharding import PartitionSpec as P

HEAD_SIZE = 128


rope_base = 500000.0


def slot_table(slot_ids, doc_len, doc_shard, doc_slot, capacity):
    doc_ids = jnp.arange(doc_len.shape[0], dtype=jnp.int32)
    starts = jnp.sum(jnp.where(doc_ids[None, :] < doc_ids[:, None], doc_len[None, :], 0), axis=1)
    shard_of = slot_ids // capacity
    local = slot_ids % capacity
    offset = local[:, None] - doc_slot[None, :]
    match = (
        (shard_of[:, None] == doc_shard[None, :]) & (offset >= 0) & (offset < doc_len[None, :])
    )
    filled = jnp.any(match, axis=1)
    position = jnp.sum(jnp.where(match, offset, 0), axis=1)
    source = jnp.sum(jnp.where(match, starts[None, :] + offset, 0), axis=1)
    doc_of = jnp.sum(jnp.where(match, doc_ids[None, :], 0), axis=1)
    slot_doc = jnp.where(filled, doc_of, -1 - slot_ids)
    return (source, filled, slot_doc, position)


def apply_rotary(values, positions):
    head_dim = values.shape[-1]
    half = head_dim // 2
    freq = jnp.power(
        jnp.float32(rope_base), -jnp.arange(half, dtype=jnp.float32) * (2.0 / head_dim)
    )
    angle = positions.astype(jnp.float32)[:, None] * freq[None, :]
    cosine = jnp.cos(angle)[:, None, :]
    sine = jnp.sin(angle)[:, None, :]
    lower = values[..., :half]
    upper = values[..., half:]
    return jnp.concatenate([lower * cosine - upper * sine, upper * cosine + lower * sine], axis=-1)


def attend(query_matrix, key, value_matrix, slot_doc, slot_position_index):
    scale = query_matrix.shape[-1] ** (-0.5)
    scores = (
        jnp.einsum("qgjd,kgd->gjqk", query_matrix, key, preferred_element_type=jnp.float32) * scale
    )
    allowed = (slot_doc[:, None] == slot_doc[None, :]) & (
        slot_position_index[None, :] <= slot_position_index[:, None]
    )
    scores = jnp.where(allowed[None, None], scores, -jnp.inf)
    peak = jnp.max(scores, axis=-1, keepdims=True)
    expo = jnp.exp(scores - peak)
    total = jnp.sum(expo, axis=-1)
    weights = expo.astype(jnp.bfloat16)
    mixed = jnp.einsum("gjqk,kgd->qgjd", weights, value_matrix, preferred_element_type=jnp.float32)
    result = mixed / jnp.transpose(total, (2, 0, 1))[..., None]
    return result.astype(jnp.bfloat16)


def body(tokens, wq, wk, wv, doc_len, doc_shard, doc_slot):
    shards = lax.axis_size("ctx")
    total_tokens = tokens.shape[0]
    per_shard = total_tokens // shards
    capacity = per_shard + per_shard // 2
    slot_total = capacity * shards
    q_cols = wq.shape[1]
    key_value_columns = wk.shape[1]
    members = HEAD_SIZE // key_value_columns
    groups = [
        list(range(g * members, (g + 1) * members))
        for g in range(lax.axis_size("tp") // members)
    ]

    source, filled, _, _ = slot_table(
        jnp.arange(slot_total, dtype=jnp.int32), doc_len, doc_shard, doc_slot, capacity
    )
    token_ids = jnp.arange(total_tokens, dtype=jnp.int32)
    source = jnp.where(filled, source, -1)
    placement = (
        source.astype(jnp.float32)[:, None] == token_ids.astype(jnp.float32)[None, :]
    ).astype(jnp.bfloat16)

    def placed(weights):
        term = lax.optimization_barrier(
            jnp.dot(tokens, weights, preferred_element_type=jnp.float32).astype(jnp.bfloat16)
        )
        return jnp.einsum(
            "jf,csj->cfs",
            term,
            placement.reshape(shards, capacity, total_tokens),
            preferred_element_type=jnp.float32,
        ).astype(jnp.bfloat16)

    kv_received = lax.all_to_all(placed(jnp.concatenate([wk, wv], axis=1)), "ctx", 0, 0, tiled=False)
    q_received = lax.all_to_all(placed(wq), "ctx", 0, 0, tiled=False)
    kv_summed = lax.optimization_barrier(jnp.sum(kv_received.astype(jnp.float32), axis=0))
    pieces = lax.all_gather(
        jnp.transpose(kv_summed).astype(jnp.bfloat16), "tp", axis=0, axis_index_groups=groups
    )
    q_summed = jnp.transpose(jnp.sum(q_received.astype(jnp.float32), axis=0))
    key_unrotated = jnp.transpose(pieces[:, :, :key_value_columns], (1, 0, 2)).reshape(capacity, HEAD_SIZE)
    value_matrix = jnp.transpose(pieces[:, :, key_value_columns:], (1, 0, 2)).reshape(capacity, HEAD_SIZE)

    shard = lax.axis_index("ctx")
    my_slots = shard * capacity + jnp.arange(capacity, dtype=jnp.int32)
    _, _, my_doc, my_pos = slot_table(my_slots, doc_len, doc_shard, doc_slot, capacity)
    heads_here = q_cols // HEAD_SIZE
    query_matrix = apply_rotary(
        q_summed.reshape(capacity, heads_here, HEAD_SIZE), my_pos
    ).astype(jnp.bfloat16)
    key = apply_rotary(key_unrotated.astype(jnp.float32)[:, None, :], my_pos).astype(jnp.bfloat16)
    result = attend(
        query_matrix.reshape(capacity, 1, heads_here, HEAD_SIZE),
        key,
        value_matrix[:, None, :],
        my_doc,
        my_pos,
    )
    return result.reshape(capacity, heads_here * HEAD_SIZE)


def solution(mesh):
    return jax.shard_map(
        body,
        mesh=mesh,
        in_specs=(P(None, "ctx"), P("ctx", "tp"), P("ctx", "tp"), P("ctx", "tp"), P(), P(), P()),
        out_specs=P("ctx", "tp"),
        check_vma=False,
    )
```

```python
import jax
import jax.numpy as jnp
from jax import lax
from jax.sharding import PartitionSpec as P

HEAD_SIZE = 128


rope_base = 500000.0


def slot_table(slot_ids, doc_len, doc_shard, doc_slot, capacity):
    doc_ids = jnp.arange(doc_len.shape[0], dtype=jnp.int32)
    starts = jnp.sum(jnp.where(doc_ids[None, :] < doc_ids[:, None], doc_len[None, :], 0), axis=1)
    shard_of = slot_ids // capacity
    local = slot_ids % capacity
    offset = local[:, None] - doc_slot[None, :]
    match = (
        (shard_of[:, None] == doc_shard[None, :]) & (offset >= 0) & (offset < doc_len[None, :])
    )
    filled = jnp.any(match, axis=1)
    position = jnp.sum(jnp.where(match, offset, 0), axis=1)
    source = jnp.sum(jnp.where(match, starts[None, :] + offset + 1, 0), axis=1) - 1
    doc_of = jnp.sum(jnp.where(match, doc_ids[None, :], 0), axis=1)
    slot_doc = jnp.where(filled, doc_of, -1 - slot_ids)
    return (source, filled, slot_doc, position)


def apply_rotary(values, positions):
    head_dim = values.shape[-1]
    half = head_dim // 2
    freq = jnp.power(
        jnp.float32(rope_base), -jnp.arange(half, dtype=jnp.float32) * (2.0 / head_dim)
    )
    angle = positions.astype(jnp.float32)[:, None] * freq[None, :]
    cosine = jnp.cos(angle)[:, None, :]
    sine = jnp.sin(angle)[:, None, :]
    lower = values[..., :half]
    upper = values[..., half:]
    return jnp.concatenate([lower * cosine - upper * sine, upper * cosine + lower * sine], axis=-1)


def attend(query_matrix, key, value_matrix, slot_doc, slot_position_index):
    scale = query_matrix.shape[-1] ** (-0.5)
    scores = (
        jnp.einsum("qgjd,kgd->gjqk", query_matrix, key, preferred_element_type=jnp.float32) * scale
    )
    allowed = (slot_doc[:, None] == slot_doc[None, :]) & (
        slot_position_index[None, :] <= slot_position_index[:, None]
    )
    scores = jnp.where(allowed[None, None], scores, -jnp.inf)
    peak = jnp.max(scores, axis=-1, keepdims=True)
    expo = jnp.exp(scores - peak)
    total = jnp.sum(expo, axis=-1)
    weights = expo.astype(jnp.bfloat16)
    mixed = jnp.einsum("gjqk,kgd->qgjd", weights, value_matrix, preferred_element_type=jnp.float32)
    result = mixed / jnp.transpose(total, (2, 0, 1))[..., None]
    return result.astype(jnp.bfloat16)


def body(tokens, wq, wk, wv, doc_len, doc_shard, doc_slot):
    shards = lax.axis_size("ctx")
    total_tokens = tokens.shape[0]
    per_shard = total_tokens // shards
    capacity = per_shard + per_shard // 2
    slot_total = capacity * shards
    q_cols = wq.shape[1]
    key_value_columns = wk.shape[1]
    members = HEAD_SIZE // key_value_columns
    groups = [
        list(range(g * members, (g + 1) * members))
        for g in range(lax.axis_size("tp") // members)
    ]

    source, _, _, _ = slot_table(
        jnp.arange(slot_total, dtype=jnp.int32), doc_len, doc_shard, doc_slot, capacity
    )
    token_ids = jnp.arange(total_tokens, dtype=jnp.int32)
    placement = (
        source.astype(jnp.float32)[:, None] == token_ids.astype(jnp.float32)[None, :]
    ).astype(jnp.bfloat16)

    def placed(weights):
        term = lax.optimization_barrier(
            jnp.dot(tokens, weights, preferred_element_type=jnp.float32).astype(jnp.bfloat16)
        )
        return jnp.einsum(
            "jf,csj->cfs",
            term,
            placement.reshape(shards, capacity, total_tokens),
            preferred_element_type=jnp.float32,
        ).astype(jnp.bfloat16)

    kv_received = lax.all_to_all(placed(jnp.concatenate([wk, wv], axis=1)), "ctx", 0, 0, tiled=False)
    q_received = lax.all_to_all(placed(wq), "ctx", 0, 0, tiled=False)
    kv_summed = lax.optimization_barrier(jnp.sum(kv_received.astype(jnp.float32), axis=0))
    pieces = lax.all_gather(
        jnp.transpose(kv_summed).astype(jnp.bfloat16), "tp", axis=0, axis_index_groups=groups
    )
    q_summed = jnp.transpose(jnp.sum(q_received.astype(jnp.float32), axis=0))
    key_unrotated = jnp.transpose(pieces[:, :, :key_value_columns], (1, 0, 2)).reshape(capacity, HEAD_SIZE)
    value_matrix = jnp.transpose(pieces[:, :, key_value_columns:], (1, 0, 2)).reshape(capacity, HEAD_SIZE)

    shard = lax.axis_index("ctx")
    my_slots = shard * capacity + jnp.arange(capacity, dtype=jnp.int32)
    _, _, my_doc, my_pos = slot_table(my_slots, doc_len, doc_shard, doc_slot, capacity)
    heads_here = q_cols // HEAD_SIZE
    query_matrix = apply_rotary(
        q_summed.reshape(capacity, heads_here, HEAD_SIZE), my_pos
    ).astype(jnp.bfloat16)
    key = apply_rotary(key_unrotated.astype(jnp.float32)[:, None, :], my_pos).astype(jnp.bfloat16)
    result = attend(
        query_matrix.reshape(capacity, 1, heads_here, HEAD_SIZE),
        key,
        value_matrix[:, None, :],
        my_doc,
        my_pos,
    )
    return result.reshape(capacity, heads_here * HEAD_SIZE)


def solution(mesh):
    return jax.shard_map(
        body,
        mesh=mesh,
        in_specs=(P(None, "ctx"), P("ctx", "tp"), P("ctx", "tp"), P("ctx", "tp"), P(), P(), P()),
        out_specs=P("ctx", "tp"),
        check_vma=False,
    )
```

```python
import jax
import jax.numpy as jnp
from jax import lax
from jax.sharding import PartitionSpec as P

HEAD_SIZE = 128


rope_base = 500000.0


def slot_table(slot_ids, doc_len, doc_shard, doc_slot, capacity):
    doc_ids = jnp.arange(doc_len.shape[0], dtype=jnp.int32)
    starts = jnp.sum(jnp.where(doc_ids[None, :] < doc_ids[:, None], doc_len[None, :], 0), axis=1)
    shard_of = slot_ids // capacity
    local = slot_ids % capacity
    offset = local[:, None] - doc_slot[None, :]
    match = (
        (shard_of[:, None] == doc_shard[None, :]) & (offset >= 0) & (offset < doc_len[None, :])
    )
    filled = jnp.any(match, axis=1)
    position = jnp.sum(jnp.where(match, offset, 0), axis=1)
    source = jnp.sum(jnp.where(match, starts[None, :] + offset + 1, 0), axis=1) - 1
    doc_of = jnp.sum(jnp.where(match, doc_ids[None, :], 0), axis=1)
    slot_doc = jnp.where(filled, doc_of, -1 - slot_ids)
    return (source, filled, slot_doc, position)


def apply_rotary(values, positions):
    head_dim = values.shape[-1]
    half = head_dim // 2
    freq = jnp.power(
        jnp.float32(rope_base), -jnp.arange(half, dtype=jnp.float32) * (2.0 / head_dim)
    )
    angle = positions.astype(jnp.float32)[:, None] * freq[None, :]
    cosine = jnp.cos(angle)[:, None, :]
    sine = jnp.sin(angle)[:, None, :]
    lower = values[..., :half]
    upper = values[..., half:]
    return jnp.concatenate([lower * cosine - upper * sine, upper * cosine + lower * sine], axis=-1)


def attend(query_matrix, key, value_matrix, slot_doc, slot_position_index):
    heads = query_matrix.shape[1]
    scale = query_matrix.shape[-1] ** (-0.5)
    scores = jnp.einsum("qjd,kd->qjk", query_matrix, key, preferred_element_type=jnp.float32) * scale
    allowed = (slot_doc[:, None] == slot_doc[None, :]) & (
        slot_position_index[None, :] <= slot_position_index[:, None]
    )
    scores = jnp.where(allowed[:, None, :], scores, -jnp.inf)
    peak = jnp.max(scores, axis=-1, keepdims=True)
    expo = jnp.exp(scores - peak)
    total = jnp.sum(expo, axis=-1)
    weights = expo.astype(jnp.bfloat16).reshape(expo.shape[0], -1)
    diagonal = jnp.eye(heads, dtype=value_matrix.dtype)
    spread = (diagonal[:, None, :, None] * value_matrix[None, :, None, :]).reshape(
        heads * value_matrix.shape[0], heads * value_matrix.shape[1]
    )
    mixed = jnp.dot(weights, spread, preferred_element_type=jnp.float32)
    result = mixed / jnp.repeat(total, value_matrix.shape[1], axis=1)
    return result.astype(jnp.bfloat16)


def body(tokens, wq, wk, wv, doc_len, doc_shard, doc_slot):
    shards = lax.axis_size("ctx")
    total_tokens = tokens.shape[0]
    per_shard = total_tokens // shards
    capacity = per_shard + per_shard // 2
    slot_total = capacity * shards
    q_cols = wq.shape[1]
    key_value_columns = wk.shape[1]
    members = HEAD_SIZE // key_value_columns
    groups = [
        list(range(g * members, (g + 1) * members))
        for g in range(lax.axis_size("tp") // members)
    ]

    source, _, _, _ = slot_table(
        jnp.arange(slot_total, dtype=jnp.int32), doc_len, doc_shard, doc_slot, capacity
    )
    token_ids = jnp.arange(total_tokens, dtype=jnp.int32)
    placement = (
        source.astype(jnp.float32)[:, None] == token_ids.astype(jnp.float32)[None, :]
    ).astype(jnp.bfloat16)

    def placed(weights):
        term = lax.optimization_barrier(
            jnp.dot(tokens, weights, preferred_element_type=jnp.float32).astype(jnp.bfloat16)
        )
        return jnp.einsum(
            "jf,csj->cfs",
            term,
            placement.reshape(shards, capacity, total_tokens),
            preferred_element_type=jnp.float32,
        ).astype(jnp.bfloat16)

    kv_received = lax.all_to_all(placed(jnp.concatenate([wk, wv], axis=1)), "ctx", 0, 0, tiled=False)
    q_received = lax.all_to_all(placed(wq), "ctx", 0, 0, tiled=False)
    kv_summed = lax.optimization_barrier(jnp.sum(kv_received.astype(jnp.float32), axis=0))
    pieces = lax.all_gather(
        jnp.transpose(kv_summed).astype(jnp.bfloat16), "tp", axis=0, axis_index_groups=groups
    )
    q_summed = jnp.transpose(jnp.sum(q_received.astype(jnp.float32), axis=0))
    key_unrotated = jnp.transpose(pieces[:, :, :key_value_columns], (1, 0, 2)).reshape(capacity, HEAD_SIZE)
    value_matrix = jnp.transpose(pieces[:, :, key_value_columns:], (1, 0, 2)).reshape(capacity, HEAD_SIZE)

    shard = lax.axis_index("ctx")
    my_slots = shard * capacity + jnp.arange(capacity, dtype=jnp.int32)
    _, _, my_doc, my_pos = slot_table(my_slots, doc_len, doc_shard, doc_slot, capacity)
    heads_here = q_cols // HEAD_SIZE
    query_matrix = apply_rotary(
        q_summed.reshape(capacity, heads_here, HEAD_SIZE), my_pos
    ).astype(jnp.bfloat16)
    key = apply_rotary(key_unrotated.astype(jnp.float32)[:, None, :], my_pos).astype(jnp.bfloat16)
    return attend(
        query_matrix,
        key.reshape(capacity, HEAD_SIZE),
        value_matrix,
        my_doc,
        my_pos,
    )


def solution(mesh):
    return jax.shard_map(
        body,
        mesh=mesh,
        in_specs=(P(None, "ctx"), P("ctx", "tp"), P("ctx", "tp"), P("ctx", "tp"), P(), P(), P()),
        out_specs=P("ctx", "tp"),
        check_vma=False,
    )
```

```python
import jax
import jax.numpy as jnp
from jax import lax
from jax.sharding import PartitionSpec as P

HEAD_SIZE = 128


rope_base = 500000.0


def slot_table(slot_ids, doc_len, doc_shard, doc_slot, capacity):
    doc_ids = jnp.arange(doc_len.shape[0], dtype=jnp.int32)
    starts = jnp.dot(
        (doc_ids[None, :] < doc_ids[:, None]).astype(jnp.float32),
        doc_len.astype(jnp.float32),
        precision=lax.Precision.HIGHEST,
    ).astype(jnp.int32)
    shard_of = slot_ids // capacity
    local = slot_ids % capacity
    offset = local[:, None] - doc_slot[None, :]
    match = (
        (shard_of[:, None] == doc_shard[None, :]) & (offset >= 0) & (offset < doc_len[None, :])
    )
    filled = jnp.any(match, axis=1)
    position = jnp.sum(jnp.where(match, offset, 0), axis=1)
    source = jnp.sum(jnp.where(match, starts[None, :] + offset + 1, 0), axis=1) - 1
    doc_of = jnp.sum(jnp.where(match, doc_ids[None, :], 0), axis=1)
    slot_doc = jnp.where(filled, doc_of, -1 - slot_ids)
    return (source, filled, slot_doc, position)


def apply_rotary(values, positions):
    head_dim = values.shape[-1]
    half = head_dim // 2
    freq = jnp.power(
        jnp.float32(rope_base), -jnp.arange(half, dtype=jnp.float32) * (2.0 / head_dim)
    )
    angle = positions.astype(jnp.float32)[:, None] * freq[None, :]
    cosine = jnp.cos(angle)[:, None, :]
    sine = jnp.sin(angle)[:, None, :]
    lower = values[..., :half]
    upper = values[..., half:]
    return jnp.concatenate([lower * cosine - upper * sine, upper * cosine + lower * sine], axis=-1)


def attend(query_matrix, key, value_matrix, slot_doc, slot_position_index):
    heads = query_matrix.shape[1]
    scale = query_matrix.shape[-1] ** (-0.5)
    scores = jnp.einsum("qjd,kd->qjk", query_matrix, key, preferred_element_type=jnp.float32) * scale
    allowed = (slot_doc[:, None] == slot_doc[None, :]) & (
        slot_position_index[None, :] <= slot_position_index[:, None]
    )
    scores = jnp.where(allowed[:, None, :], scores, -jnp.inf)
    peak = jnp.max(scores, axis=-1, keepdims=True)
    expo = jnp.exp(scores - peak)
    total = jnp.sum(expo, axis=-1)
    weights = expo.astype(jnp.bfloat16).reshape(expo.shape[0], -1)
    diagonal = jnp.eye(heads, dtype=value_matrix.dtype)
    spread = (diagonal[:, None, :, None] * value_matrix[None, :, None, :]).reshape(
        heads * value_matrix.shape[0], heads * value_matrix.shape[1]
    )
    mixed = jnp.dot(weights, spread, preferred_element_type=jnp.float32)
    result = mixed / jnp.repeat(total, value_matrix.shape[1], axis=1)
    return result.astype(jnp.bfloat16)


def body(tokens, wq, wk, wv, doc_len, doc_shard, doc_slot):
    shards = lax.axis_size("ctx")
    total_tokens = tokens.shape[0]
    per_shard = total_tokens // shards
    capacity = per_shard + per_shard // 2
    slot_total = capacity * shards
    q_cols = wq.shape[1]
    key_value_columns = wk.shape[1]
    members = HEAD_SIZE // key_value_columns
    groups = [
        list(range(g * members, (g + 1) * members))
        for g in range(lax.axis_size("tp") // members)
    ]

    source, _, _, _ = slot_table(
        jnp.arange(slot_total, dtype=jnp.int32), doc_len, doc_shard, doc_slot, capacity
    )
    token_ids = jnp.arange(total_tokens, dtype=jnp.int32)
    placement = (
        source.astype(jnp.float32)[:, None] == token_ids.astype(jnp.float32)[None, :]
    ).astype(jnp.bfloat16)

    def placed(weights):
        term = lax.optimization_barrier(
            jnp.dot(tokens, weights, preferred_element_type=jnp.float32).astype(jnp.bfloat16)
        )
        return jnp.einsum(
            "jf,csj->cfs",
            term,
            placement.reshape(shards, capacity, total_tokens),
            preferred_element_type=jnp.float32,
        ).astype(jnp.bfloat16)

    kv_received = lax.all_to_all(placed(jnp.concatenate([wk, wv], axis=1)), "ctx", 0, 0, tiled=False)
    q_received = lax.all_to_all(placed(wq), "ctx", 0, 0, tiled=False)
    kv_summed = lax.optimization_barrier(jnp.sum(kv_received.astype(jnp.float32), axis=0))
    pieces = lax.all_gather(
        jnp.transpose(kv_summed).astype(jnp.bfloat16), "tp", axis=0, axis_index_groups=groups
    )
    q_summed = jnp.transpose(jnp.sum(q_received.astype(jnp.float32), axis=0))
    key_unrotated = jnp.transpose(pieces[:, :, :key_value_columns], (1, 0, 2)).reshape(capacity, HEAD_SIZE)
    value_matrix = jnp.transpose(pieces[:, :, key_value_columns:], (1, 0, 2)).reshape(capacity, HEAD_SIZE)

    shard = lax.axis_index("ctx")
    my_slots = shard * capacity + jnp.arange(capacity, dtype=jnp.int32)
    _, _, my_doc, my_pos = slot_table(my_slots, doc_len, doc_shard, doc_slot, capacity)
    heads_here = q_cols // HEAD_SIZE
    query_matrix = apply_rotary(
        q_summed.reshape(capacity, heads_here, HEAD_SIZE), my_pos
    ).astype(jnp.bfloat16)
    key = apply_rotary(key_unrotated.astype(jnp.float32)[:, None, :], my_pos).astype(jnp.bfloat16)
    return attend(
        query_matrix,
        key.reshape(capacity, HEAD_SIZE),
        value_matrix,
        my_doc,
        my_pos,
    )


def solution(mesh):
    return jax.shard_map(
        body,
        mesh=mesh,
        in_specs=(P(None, "ctx"), P("ctx", "tp"), P("ctx", "tp"), P("ctx", "tp"), P(), P(), P()),
        out_specs=P("ctx", "tp"),
        check_vma=False,
    )
```
